256 devices in a mesh: segment: 2 (over y_lo), gx: 8 (over x, y_hi), gy: 16 (over z, core).
Axes of the slice: x: 4, y: 4 (y_hi: 2, y_lo: 2; y = y_hi * 2 + y_lo), z: 8, core: 2. Of those that a mesh axis runs over, the one named last changes fastest.
Arguments:
- node_latent: bfloat16 [131072, 512], P(('segment', 'gx', 'gy')), may hold values from -6 to 6
- edge_latent: bfloat16 [262144, 512], P(('segment', 'gx', 'gy')), may hold values from -6 to 6
- adjacency: bfloat16 [1024, 2, 128, 128], P(('segment', 'gx', 'gy')), may hold values from -0.5 to 0.5
- neighbours: int32 [1024, 2], P(('segment', 'gx', 'gy')), may hold values from 0 to 9, as said below
- live: int32 [1024, 2], P(('segment', 'gx', 'gy')), may hold values 0 or 1
- send_blocks: int32 [256, 6], P(('segment', 'gx', 'gy')), may hold values from 0 to 3
- w_edge_in: bfloat16 [1536, 512], replicated, may hold values from -0.15625 to 0.15625
- w_edge_out: bfloat16 [512, 512], replicated, may hold values from -0.25 to 0.25
- w_node_in: bfloat16 [1024, 512], replicated, may hold values from -0.1875 to 0.1875
- w_node_out: bfloat16 [512, 512], replicated, may hold values from -0.25 to 0.25
- node_cotangent: bfloat16 [131072, 512], P(('segment', 'gx', 'gy')), may hold values from -6 to 6
- edge_cotangent: bfloat16 [262144, 512], P(('segment', 'gx', 'gy')), may hold values from -6 to 6
Outputs:
- node_out: bfloat16 [131072, 512], P(('segment', 'gx', 'gy'))
- edge_out: bfloat16 [262144, 512], P(('segment', 'gx', 'gy'))
- node_grad: float32 [131072, 512], P(('segment', 'gx', 'gy'))
- grad_edge_in: float32 [786432], P(('segment', 'gx', 'gy'))
- grad_edge_out: float32 [262144], P(('segment', 'gx', 'gy'))
- grad_node_in: float32 [524288], P(('segment', 'gx', 'gy'))
- grad_node_out: float32 [262144], P(('segment', 'gx', 'gy'))
The draws below stay inside these ranges and needn't reach their ends.
Inputs may be any that keep to these rules, and one draw needn't show every extreme that they name: `neighbours`: indices below 4 name the device's own blocks, 4 + j names received block j; on every device each of the six received blocks is named by at least one slot.
All inputs are finite; a program needn't handle non-finite values. No bound on the sum of `live` on one device may be relied on, other than what follows from the above.
Results may differ from the reference program's by a relative error of at most 0.014.
Values may be sent and summed in bfloat16 or wider, within the bound.
No kernel may reach another device: no remote copies, remote signals or barrier semaphores. Data moves between devices by JAX's collectives and lax.ppermute only.
A program may use at most 128 MiB of HBM per device.

```python
from functools import partial
import jax
import jax.numpy as jnp
from jax import lax

D = 512
BLK = 128
NB = 4
K = 2
SUBDOMAINS = 256
BLOCKS = 1024
NODES = 131072
EDGE_ROWS = 262144
N_SEGMENT = 2
N_GX = 8
N_GY = 16


def draw_neighbours(key, part):
    per_device = BLOCKS // NB
    slot_count = NB * K
    first_key, second_key = jax.random.split(key)
    local_pick = jax.random.randint(first_key, (per_device, slot_count), 0, NB + 6)
    device_keys = jax.random.split(second_key, per_device)

    def shuffle_one(device_key):
        return jax.random.permutation(device_key, slot_count)
    shuffled = jax.vmap(shuffle_one)(device_keys)
    position = jnp.argsort(shuffled, axis=1, stable=True)
    chosen = jnp.where(position < 6, NB + position, local_pick)
    return chosen.reshape(BLOCKS, K).astype(jnp.int32)


def set_ends(drawn, rng, least, top_value):
    shape = drawn.shape
    index_at = [jax.random.randint(jax.random.fold_in(rng, axis), (), 0, shape[axis]) for axis in range(len(shape))]
    drawn = drawn.at[tuple(index_at)].set(least)
    longest = shape.index(max(shape))
    index_at[longest] = (index_at[longest] + 1) % shape[longest]
    return drawn.at[tuple(index_at)].set(top_value)


def steps_of(stream_key, shape, cuts, low, top_value):
    factor_of, own = 1.0, jax.random.fold_in(stream_key, 6)
    for axis_at, blocks in cuts:
        steps = jnp.exp(jax.random.uniform(jax.random.fold_in(own, axis_at), (blocks,), jnp.float32, low / len(cuts), top_value / len(cuts)))
        factor_of = factor_of * jnp.repeat(steps, shape[axis_at] // blocks).reshape([-1 if axis == axis_at else 1 for axis in range(len(shape))])
    return factor_of


def normal_values(key, shape, deviation, most, cuts=(), dtype=jnp.bfloat16):
    values = jax.random.normal(key, shape, jnp.float32) * deviation
    if len(cuts) > 0:
        values = steps_of(key, shape, cuts, -0.22, 0.18) * values
    return jnp.clip(values, min=-most, max=most).astype(dtype)


def setup_inputs(seed: int = 0) -> dict:
    streams_of = jax.random.split(jax.random.key(seed), 13)
    return {
        "node_latent": normal_values(streams_of[0], (NODES, D), 1.0, 6.0, ((0, 256),)),
        "edge_latent": normal_values(streams_of[1], (EDGE_ROWS, D), 1.0, 6.0, ((0, 256),)),
        "adjacency": normal_values(streams_of[2], (BLOCKS, K, BLK, BLK), BLK ** -0.5, 0.5, ((0, 256),)),
        "neighbours": draw_neighbours(jax.random.fold_in(streams_of[12], 71), 0),
        "live": set_ends((jax.random.randint(streams_of[4], (BLOCKS, K), 0, 4) < 3).astype(jnp.int32), jax.random.fold_in(streams_of[4], 1), 0, 1),
        "send_blocks": set_ends(jax.random.randint(streams_of[5], (SUBDOMAINS, 6), 0, NB), jax.random.fold_in(streams_of[5], 1), 0, NB - 1).astype(jnp.int32),
        "w_edge_in": normal_values(streams_of[6], (3 * D, D), (3 * D) ** -0.5, 0.15625),
        "w_edge_out": normal_values(streams_of[7], (D, D), D ** -0.5, 0.25),
        "w_node_in": normal_values(streams_of[8], (2 * D, D), (2 * D) ** -0.5, 0.1875),
        "w_node_out": normal_values(streams_of[9], (D, D), D ** -0.5, 0.25),
        "node_cotangent": normal_values(streams_of[10], (NODES, D), 1.0, 6.0, ((0, 256),)),
        "edge_cotangent": normal_values(streams_of[11], (EDGE_ROWS, D), 1.0, 6.0, ((0, 256),)),
    }


def layer_norm(values):
    average = lax.optimization_barrier(jnp.mean(values, axis=-1, keepdims=True))
    centred = values - average
    return centred * lax.rsqrt(lax.optimization_barrier(jnp.mean(centred * centred, axis=-1, keepdims=True)) + 1e-05)

def edge_part(node_blocks, received, w_edge_in, w_edge_out, edge_rows, adjacency_tiles, picker):
    latent = node_blocks.shape[-1]
    blocks = node_blocks.shape[0]
    block_rows = node_blocks.shape[1]
    degree = picker.shape[0] // blocks
    extended = jnp.concatenate([node_blocks, received], axis=0)
    sources = jnp.einsum('sn,nbd->sbd', picker.astype(jnp.float32), extended.astype(jnp.float32)).astype(jnp.bfloat16)
    mixed_rows = jnp.einsum('sij,sjd->sid', adjacency_tiles.astype(jnp.float32), sources.astype(jnp.float32)).astype(jnp.bfloat16)
    self_term = jnp.dot(node_blocks.reshape(-1, latent), w_edge_in[latent:2 * latent], preferred_element_type=jnp.float32)
    pre_edge = jnp.dot(edge_rows, w_edge_in[:latent], preferred_element_type=jnp.float32) + jnp.dot(mixed_rows.reshape(-1, latent), w_edge_in[2 * latent:], preferred_element_type=jnp.float32)
    pre_edge = (pre_edge.reshape(blocks, degree, block_rows, latent) + self_term.reshape(blocks, 1, block_rows, latent)).reshape(-1, latent)
    edge_hidden = jax.nn.silu(pre_edge).astype(jnp.bfloat16)
    return layer_norm(jnp.dot(edge_hidden, w_edge_out, preferred_element_type=jnp.float32))

def node_part(node_blocks, messages, w_node_in, w_node_out, edge_rows, live_weight):
    latent = node_blocks.shape[-1]
    blocks = node_blocks.shape[0]
    block_rows = node_blocks.shape[1]
    edges_out = (edge_rows.astype(jnp.float32) + messages).astype(jnp.bfloat16)
    gathered = lax.optimization_barrier(jnp.sum(messages.reshape(blocks, -1, block_rows, latent) * live_weight[:, :, None, None], axis=1)).astype(jnp.bfloat16)
    flat_nodes = node_blocks.reshape(-1, latent)
    pre_node = jnp.dot(flat_nodes, w_node_in[:latent], preferred_element_type=jnp.float32) + jnp.dot(gathered.reshape(-1, latent), w_node_in[latent:], preferred_element_type=jnp.float32)
    node_hidden = jax.nn.silu(pre_node).astype(jnp.bfloat16)
    nodes_out = (flat_nodes.astype(jnp.float32) + layer_norm(jnp.dot(node_hidden, w_node_out, preferred_element_type=jnp.float32))).astype(jnp.bfloat16)
    return (nodes_out, edges_out)

def shift_grid(blocks, axis, offset):
    extent = blocks.shape[axis]
    zero_layer = jnp.zeros_like(lax.slice_in_dim(blocks, 0, 1, axis=axis))
    if offset > 0:
        return jnp.concatenate([zero_layer, lax.slice_in_dim(blocks, 0, extent - 1, axis=axis)], axis=axis)
    return jnp.concatenate([lax.slice_in_dim(blocks, 1, extent, axis=axis), zero_layer], axis=axis)

def exchange_grid(faces_grid):
    pieces = [shift_grid(faces_grid[:, :, :, 1], 1, 1), shift_grid(faces_grid[:, :, :, 0], 1, -1), shift_grid(faces_grid[:, :, :, 3], 2, 1), shift_grid(faces_grid[:, :, :, 2], 2, -1), shift_grid(faces_grid[:, :, :, 5], 0, 1), shift_grid(faces_grid[:, :, :, 4], 0, -1)]
    return jnp.stack(pieces, axis=3)

def reference(node_latent, edge_latent, adjacency, neighbours, live, send_blocks, w_edge_in, w_edge_out, w_node_in, w_node_out, node_cotangent, edge_cotangent):
    devices = N_SEGMENT * N_GX * N_GY
    latent = node_latent.shape[1]
    node_grid = node_latent.reshape(N_SEGMENT, N_GX, N_GY, NB, BLK, latent)
    choose = (send_blocks.reshape(N_SEGMENT, N_GX, N_GY, 6)[..., None] == jnp.arange(NB).astype(jnp.int32)).astype(jnp.float32)
    outgoing = jnp.einsum('sxyjn,sxynbd->sxyjbd', choose, node_grid.astype(jnp.float32)).astype(jnp.bfloat16)
    received = exchange_grid(outgoing).reshape(devices, 6, BLK, latent)
    device_items = (node_latent.reshape(devices, NB, BLK, latent), received, edge_latent.reshape(devices, NB * K * BLK, latent), adjacency.reshape(devices, NB * K, BLK, BLK), neighbours.reshape(devices, NB * K), live.reshape(devices, NB, K), node_cotangent.reshape(devices, NB * BLK, latent), edge_cotangent.reshape(devices, NB * K * BLK, latent))

    def visit_device(totals, items):
        node_blocks, recv_blocks, edge_rows, adjacency_tiles, slot_names, live_mask, node_ct, edge_ct = items
        picker = (slot_names[:, None] == jnp.arange(NB + 6).astype(jnp.int32)[None, :]).astype(jnp.bfloat16)
        live_weight = live_mask.astype(jnp.float32)
        messages, edge_pull = jax.vjp(partial(edge_part, edge_rows=edge_rows, adjacency_tiles=adjacency_tiles, picker=picker), node_blocks, recv_blocks, w_edge_in, w_edge_out)
        outputs, node_pull = jax.vjp(partial(node_part, edge_rows=edge_rows, live_weight=live_weight), node_blocks, messages, w_node_in, w_node_out)
        node_direct, message_ct, grad_ni, grad_no = node_pull((node_ct, edge_ct))
        node_indirect, received_ct, grad_ei, grad_eo = edge_pull(message_ct)
        terms = (grad_ei, grad_eo, grad_ni, grad_no)
        totals = tuple((total + term.astype(jnp.float32) for total, term in zip(totals, terms)))
        local_grad = node_direct.astype(jnp.float32) + node_indirect.astype(jnp.float32)
        return (totals, (outputs[0], outputs[1], local_grad, received_ct))
    start = tuple((jnp.zeros(weight.shape, jnp.float32) for weight in (w_edge_in, w_edge_out, w_node_in, w_node_out)))
    totals, stacked = lax.scan(visit_device, start, device_items)
    nodes_out, edges_out, local_grad, received_ct = stacked
    returned = exchange_grid(received_ct.reshape(N_SEGMENT, N_GX, N_GY, 6, BLK, latent))
    node_grad = local_grad.reshape(N_SEGMENT, N_GX, N_GY, NB, BLK, latent) + jnp.einsum('sxyjn,sxyjbd->sxynbd', choose, returned.astype(jnp.float32))
    return (nodes_out.reshape(-1, latent), edges_out.reshape(-1, latent), node_grad.reshape(-1, latent), totals[0].reshape(-1), totals[1].reshape(-1), totals[2].reshape(-1), totals[3].reshape(-1))
```

```python
from functools import partial

import jax
import jax.numpy as jnp
from jax import lax
from jax.sharding import PartitionSpec as P


def passed_along(block, axis, distance):
    devices = range(lax.axis_size(axis))
    route = [(i - distance, i) for i in devices if i - distance in devices]
    return lax.ppermute(block, axis, route)


INDEX_BITS = (("segment", 0), ("gx", 2), ("gx", 1), ("gx", 0), ("gy", 3), ("gy", 2), ("gy", 1), ("gy", 0))
EDGE_IN_ORDER = (7, 0, 6, 2, 5, 3, 1, 4)
EDGE_OUT_ORDER = (7, 2, 0, 6, 1, 5, 3, 4)
NODE_IN_ORDER = (7, 6, 2, 0, 3, 5, 4, 1)
NODE_OUT_ORDER = (7, 2, 0, 6, 1, 5, 3, 4)


def halving_scatter(flat, order):
    devices = 1 << len(INDEX_BITS)
    share = flat.shape[0] // devices
    parts = flat.reshape((2,) * len(INDEX_BITS) + (share,)).transpose(tuple(order) + (len(INDEX_BITS),))
    for position in order:
        axis, bit = INDEX_BITS[position]
        side = (lax.axis_index(axis) >> bit) & 1
        route = [(j, j ^ (1 << bit)) for j in range(lax.axis_size(axis))]
        keep = lax.dynamic_index_in_dim(parts, side, 0, keepdims=False)
        send = lax.dynamic_index_in_dim(parts, 1 - side, 0, keepdims=False)
        parts = keep + lax.ppermute(send, axis, route)
    return parts


def layer_norm(values):
    average = jnp.mean(values, axis=-1, keepdims=True)
    centred = values - average
    return centred * lax.rsqrt(jnp.mean(centred * centred, axis=-1, keepdims=True) + 1e-05)


def edge_part(node_blocks, received, w_edge_in, w_edge_out, edge_rows, adjacency_tiles, picker):
    latent = node_blocks.shape[-1]
    blocks = node_blocks.shape[0]
    block_rows = node_blocks.shape[1]
    degree = picker.shape[0] // blocks
    extended = jnp.concatenate([node_blocks, received], axis=0)
    sources = jnp.einsum(
        "sn,nbd->sbd", picker, extended, preferred_element_type=jnp.float32
    ).astype(jnp.bfloat16)
    mixed_rows = jnp.einsum(
        "sij,sjd->sid", adjacency_tiles, sources, preferred_element_type=jnp.float32
    ).astype(jnp.bfloat16)
    self_term = jnp.dot(
        node_blocks.reshape(-1, latent),
        w_edge_in[latent : 2 * latent],
        preferred_element_type=jnp.float32,
    )
    pre_edge = jnp.dot(edge_rows, w_edge_in[:latent], preferred_element_type=jnp.float32) + jnp.dot(
        mixed_rows.reshape(-1, latent), w_edge_in[2 * latent :], preferred_element_type=jnp.float32
    )
    pre_edge = (
        pre_edge.reshape(blocks, degree, block_rows, latent)
        + self_term.reshape(blocks, 1, block_rows, latent)
    ).reshape(-1, latent)
    edge_hidden = jax.nn.silu(pre_edge).astype(jnp.bfloat16)
    return layer_norm(jnp.dot(edge_hidden, w_edge_out, preferred_element_type=jnp.float32))


def node_part(node_blocks, messages, w_node_in, w_node_out, edge_rows, live_weight):
    latent = node_blocks.shape[-1]
    blocks = node_blocks.shape[0]
    block_rows = node_blocks.shape[1]
    edges_out = (edge_rows.astype(jnp.float32) + messages).astype(jnp.bfloat16)
    gathered = jnp.sum(
        messages.reshape(blocks, -1, block_rows, latent) * live_weight[:, :, None, None], axis=1
    ).astype(jnp.bfloat16)
    flat_nodes = node_blocks.reshape(-1, latent)
    pre_node = jnp.dot(
        flat_nodes, w_node_in[:latent], preferred_element_type=jnp.float32
    ) + jnp.dot(
        gathered.reshape(-1, latent), w_node_in[latent:], preferred_element_type=jnp.float32
    )
    node_hidden = jax.nn.silu(pre_node).astype(jnp.bfloat16)
    nodes_out = (
        flat_nodes.astype(jnp.float32)
        + layer_norm(jnp.dot(node_hidden, w_node_out, preferred_element_type=jnp.float32))
    ).astype(jnp.bfloat16)
    return (nodes_out, edges_out)


def across_rows(face_rows, offset):
    return passed_along(face_rows, "gx", offset)


def across_cols(face_rows, offset):
    return passed_along(face_rows, "gy", offset)


def across_segment(face_rows, offset):
    return passed_along(face_rows, "segment", offset)


def swap_faces(face_blocks):
    return jnp.stack(
        [
            across_rows(face_blocks[1], 1),
            across_rows(face_blocks[0], -1),
            across_cols(face_blocks[3], 1),
            across_cols(face_blocks[2], -1),
            across_segment(face_blocks[5], 1),
            across_segment(face_blocks[4], -1),
        ],
        axis=0,
    )


def shards(
    node_latent,
    edge_latent,
    adjacency,
    neighbours,
    live,
    send_blocks,
    w_edge_in,
    w_edge_out,
    w_node_in,
    w_node_out,
    node_cotangent,
    edge_cotangent,
):
    latent = node_latent.shape[1]
    blocks, degree = neighbours.shape
    block_rows = adjacency.shape[-1]
    node_blocks = node_latent.reshape(blocks, block_rows, latent)
    choose = (send_blocks[0][:, None] == jnp.arange(blocks, dtype=jnp.int32)[None, :]).astype(
        jnp.bfloat16
    )
    outgoing = jnp.einsum(
        "jn,nbd->jbd", choose, node_blocks, preferred_element_type=jnp.float32
    ).astype(jnp.bfloat16)
    received = swap_faces(outgoing)
    adjacency_tiles = adjacency.reshape(blocks * degree, block_rows, block_rows)
    picker = (
        neighbours.reshape(-1)[:, None] == jnp.arange(blocks + 6, dtype=jnp.int32)[None, :]
    ).astype(jnp.bfloat16)
    live_weight = live.astype(jnp.float32)
    messages, edge_pull = jax.vjp(
        partial(edge_part, edge_rows=edge_latent, adjacency_tiles=adjacency_tiles, picker=picker),
        node_blocks,
        received,
        w_edge_in,
        w_edge_out,
    )
    outputs, node_pull = jax.vjp(
        partial(node_part, edge_rows=edge_latent, live_weight=live_weight),
        node_blocks,
        messages,
        w_node_in,
        w_node_out,
    )
    node_direct, message_ct, grad_ni, grad_no = node_pull((node_cotangent, edge_cotangent))
    node_terms = (grad_ni.astype(jnp.float32).reshape(-1), grad_no.astype(jnp.float32).reshape(-1))
    node_indirect, received_ct, grad_ei, grad_eo = edge_pull(message_ct)
    returned = swap_faces(received_ct)
    node_grad = node_direct.astype(jnp.float32) + node_indirect.astype(jnp.float32)
    node_grad = node_grad + jnp.einsum(
        "jn,jbd->nbd", choose, returned, preferred_element_type=jnp.float32
    )
    edge_terms = (grad_ei.astype(jnp.float32).reshape(-1), grad_eo.astype(jnp.float32).reshape(-1))
    shares = (
        halving_scatter(edge_terms[0], EDGE_IN_ORDER),
        halving_scatter(edge_terms[1], EDGE_OUT_ORDER),
        halving_scatter(node_terms[0], NODE_IN_ORDER),
        halving_scatter(node_terms[1], NODE_OUT_ORDER),
    )
    return (
        outputs[0],
        outputs[1],
        node_grad.reshape(-1, latent),
        shares[0],
        shares[1],
        shares[2],
        shares[3],
    )


def solution(mesh):
    placed = (
        P(("segment", "gx", "gy"), None),
        P(("segment", "gx", "gy"), None),
        P(("segment", "gx", "gy"), None, None, None),
        P(("segment", "gx", "gy"), None),
        P(("segment", "gx", "gy"), None),
        P(("segment", "gx", "gy"), None),
        P(),
        P(),
        P(),
        P(),
        P(("segment", "gx", "gy"), None),
        P(("segment", "gx", "gy"), None),
    )
    return jax.shard_map(
        shards,
        mesh=mesh,
        in_specs=placed,
        out_specs=(
            P(("segment", "gx", "gy"), None),
            P(("segment", "gx", "gy"), None),
            P(("segment", "gx", "gy"), None),
            P(("segment", "gx", "gy")),
            P(("segment", "gx", "gy")),
            P(("segment", "gx", "gy")),
            P(("segment", "gx", "gy")),
        ),
        check_vma=False,
    )
```

```python
from functools import partial

import jax
import jax.numpy as jnp
from jax import lax
from jax.sharding import PartitionSpec as P


def passed_along(block, axis, distance):
    devices = range(lax.axis_size(axis))
    route = [(i - distance, i) for i in devices if i - distance in devices]
    return lax.ppermute(block, axis, route)


INDEX_BITS = (("segment", 0), ("gx", 2), ("gx", 1), ("gx", 0), ("gy", 3), ("gy", 2), ("gy", 1), ("gy", 0))
EDGE_ORDER = (7, 0, 6, 2, 5, 3, 1, 4)
NODE_ORDER = (7, 6, 2, 0, 3, 5, 4, 1)

def halving_scatter(rows, order):
    bits = len(INDEX_BITS)
    parts = rows.reshape((2,) * bits + rows.shape[1:]).transpose(tuple(order) + (bits,))
    for position in order:
        axis, bit = INDEX_BITS[position]
        side = (lax.axis_index(axis) >> bit) & 1
        route = [(j, j ^ (1 << bit)) for j in range(lax.axis_size(axis))]
        keep = lax.dynamic_index_in_dim(parts, side, 0, keepdims=False)
        send = lax.dynamic_index_in_dim(parts, 1 - side, 0, keepdims=False)
        parts = keep + lax.ppermute(send, axis, route)
    return parts


def layer_norm(values):
    average = jnp.mean(values, axis=-1, keepdims=True)
    centred = values - average
    return centred * lax.rsqrt(jnp.mean(centred * centred, axis=-1, keepdims=True) + 1e-05)


def edge_part(node_blocks, received, w_edge_in, w_edge_out, edge_rows, adjacency_tiles, picker):
    latent = node_blocks.shape[-1]
    blocks = node_blocks.shape[0]
    block_rows = node_blocks.shape[1]
    degree = picker.shape[0] // blocks
    extended = jnp.concatenate([node_blocks, received], axis=0)
    sources = jnp.einsum(
        "sn,nbd->sbd", picker, extended, preferred_element_type=jnp.float32
    ).astype(jnp.bfloat16)
    mixed_rows = jnp.einsum(
        "sij,sjd->sid", adjacency_tiles, sources, preferred_element_type=jnp.float32
    ).astype(jnp.bfloat16)
    self_term = jnp.dot(
        node_blocks.reshape(-1, latent),
        w_edge_in[latent : 2 * latent],
        preferred_element_type=jnp.float32,
    )
    pre_edge = jnp.dot(edge_rows, w_edge_in[:latent], preferred_element_type=jnp.float32) + jnp.dot(
        mixed_rows.reshape(-1, latent), w_edge_in[2 * latent :], preferred_element_type=jnp.float32
    )
    pre_edge = (
        pre_edge.reshape(blocks, degree, block_rows, latent)
        + self_term.reshape(blocks, 1, block_rows, latent)
    ).reshape(-1, latent)
    edge_hidden = jax.nn.silu(pre_edge).astype(jnp.bfloat16)
    return layer_norm(jnp.dot(edge_hidden, w_edge_out, preferred_element_type=jnp.float32))


def node_part(node_blocks, messages, w_node_in, w_node_out, edge_rows, live_weight):
    latent = node_blocks.shape[-1]
    blocks = node_blocks.shape[0]
    block_rows = node_blocks.shape[1]
    edges_out = (edge_rows.astype(jnp.float32) + messages).astype(jnp.bfloat16)
    gathered = jnp.sum(
        messages.reshape(blocks, -1, block_rows, latent) * live_weight[:, :, None, None], axis=1
    ).astype(jnp.bfloat16)
    flat_nodes = node_blocks.reshape(-1, latent)
    pre_node = jnp.dot(
        flat_nodes, w_node_in[:latent], preferred_element_type=jnp.float32
    ) + jnp.dot(
        gathered.reshape(-1, latent), w_node_in[latent:], preferred_element_type=jnp.float32
    )
    node_hidden = jax.nn.silu(pre_node).astype(jnp.bfloat16)
    nodes_out = (
        flat_nodes.astype(jnp.float32)
        + layer_norm(jnp.dot(node_hidden, w_node_out, preferred_element_type=jnp.float32))
    ).astype(jnp.bfloat16)
    return (nodes_out, edges_out)


def across_rows(face_rows, offset):
    return passed_along(face_rows, "gx", offset)


def across_cols(face_rows, offset):
    return passed_along(face_rows, "gy", offset)


def across_segment(face_rows, offset):
    return passed_along(face_rows, "segment", offset)


def swap_faces(face_blocks):
    return jnp.stack(
        [
            across_rows(face_blocks[1], 1),
            across_rows(face_blocks[0], -1),
            across_cols(face_blocks[3], 1),
            across_cols(face_blocks[2], -1),
            across_segment(face_blocks[5], 1),
            across_segment(face_blocks[4], -1),
        ],
        axis=0,
    )


def shards(
    node_latent,
    edge_latent,
    adjacency,
    neighbours,
    live,
    send_blocks,
    w_edge_in,
    w_edge_out,
    w_node_in,
    w_node_out,
    node_cotangent,
    edge_cotangent,
):
    latent = node_latent.shape[1]
    blocks, degree = neighbours.shape
    block_rows = adjacency.shape[-1]
    node_blocks = node_latent.reshape(blocks, block_rows, latent)
    choose = (send_blocks[0][:, None] == jnp.arange(blocks, dtype=jnp.int32)[None, :]).astype(
        jnp.bfloat16
    )
    outgoing = jnp.einsum(
        "jn,nbd->jbd", choose, node_blocks, preferred_element_type=jnp.float32
    ).astype(jnp.bfloat16)
    received = swap_faces(outgoing)
    adjacency_tiles = adjacency.reshape(blocks * degree, block_rows, block_rows)
    picker = (
        neighbours.reshape(-1)[:, None] == jnp.arange(blocks + 6, dtype=jnp.int32)[None, :]
    ).astype(jnp.bfloat16)
    live_weight = live.astype(jnp.float32)
    messages, edge_pull = jax.vjp(
        partial(edge_part, edge_rows=edge_latent, adjacency_tiles=adjacency_tiles, picker=picker),
        node_blocks,
        received,
        w_edge_in,
        w_edge_out,
    )
    outputs, node_pull = jax.vjp(
        partial(node_part, edge_rows=edge_latent, live_weight=live_weight),
        node_blocks,
        messages,
        w_node_in,
        w_node_out,
    )
    node_direct, message_ct, grad_ni, grad_no = node_pull((node_cotangent, edge_cotangent))
    node_terms = (grad_ni.astype(jnp.float32).reshape(-1), grad_no.astype(jnp.float32).reshape(-1))
    node_indirect, received_ct, grad_ei, grad_eo = edge_pull(message_ct)
    returned = swap_faces(received_ct)
    node_grad = node_direct.astype(jnp.float32) + node_indirect.astype(jnp.float32)
    node_grad = node_grad + jnp.einsum(
        "jn,jbd->nbd", choose, returned, preferred_element_type=jnp.float32
    )
    edge_terms = (grad_ei.astype(jnp.float32).reshape(-1), grad_eo.astype(jnp.float32).reshape(-1))
    devices = 1 << len(INDEX_BITS)
    edge_share = halving_scatter(
        jnp.concatenate([term.reshape(devices, -1) for term in edge_terms], axis=1), EDGE_ORDER
    )
    node_share = halving_scatter(
        jnp.concatenate([term.reshape(devices, -1) for term in node_terms], axis=1), NODE_ORDER
    )
    edge_cut = edge_terms[0].shape[0] // devices
    node_cut = node_terms[0].shape[0] // devices
    shares = (
        edge_share[:edge_cut],
        edge_share[edge_cut:],
        node_share[:node_cut],
        node_share[node_cut:],
    )
    return (
        outputs[0],
        outputs[1],
        node_grad.reshape(-1, latent),
        shares[0],
        shares[1],
        shares[2],
        shares[3],
    )


def solution(mesh):
    placed = (
        P(("segment", "gx", "gy"), None),
        P(("segment", "gx", "gy"), None),
        P(("segment", "gx", "gy"), None, None, None),
        P(("segment", "gx", "gy"), None),
        P(("segment", "gx", "gy"), None),
        P(("segment", "gx", "gy"), None),
        P(),
        P(),
        P(),
        P(),
        P(("segment", "gx", "gy"), None),
        P(("segment", "gx", "gy"), None),
    )
    return jax.shard_map(
        shards,
        mesh=mesh,
        in_specs=placed,
        out_specs=(
            P(("segment", "gx", "gy"), None),
            P(("segment", "gx", "gy"), None),
            P(("segment", "gx", "gy"), None),
            P(("segment", "gx", "gy")),
            P(("segment", "gx", "gy")),
            P(("segment", "gx", "gy")),
            P(("segment", "gx", "gy")),
        ),
        check_vma=False,
    )
```

```python
from functools import partial

import jax
import jax.numpy as jnp
from jax import lax
from jax.sharding import PartitionSpec as P


def passed_along(block, axis, distance):
    devices = range(lax.axis_size(axis))
    route = [(i - distance, i) for i in devices if i - distance in devices]
    return lax.ppermute(block, axis, route)


INDEX_BITS = (("segment", 0), ("gx", 2), ("gx", 1), ("gx", 0), ("gy", 3), ("gy", 2), ("gy", 1), ("gy", 0))
EDGE_ORDER = (7, 0, 6, 2, 5, 3, 1, 4)
NODE_ORDER = (7, 6, 2, 0, 3, 5, 4, 1)

def halving_scatter(rows, order):
    bits = len(INDEX_BITS)
    parts = rows.reshape((2,) * bits + rows.shape[1:]).transpose(tuple(order) + (bits,))
    for position in order:
        axis, bit = INDEX_BITS[position]
        side = (lax.axis_index(axis) >> bit) & 1
        route = [(j, j ^ (1 << bit)) for j in range(lax.axis_size(axis))]
        keep = lax.dynamic_index_in_dim(parts, side, 0, keepdims=False)
        send = lax.dynamic_index_in_dim(parts, 1 - side, 0, keepdims=False)
        if axis == "gy" and bit == 0:
            parts = keep + lax.ppermute(send, axis, route)
        else:
            arrived = lax.ppermute(send.astype(jnp.bfloat16), axis, route)
            parts = keep + arrived.astype(jnp.float32)
    return parts


def layer_norm(values):
    average = jnp.mean(values, axis=-1, keepdims=True)
    centred = values - average
    return centred * lax.rsqrt(jnp.mean(centred * centred, axis=-1, keepdims=True) + 1e-05)


def edge_part(node_blocks, received, w_edge_in, w_edge_out, edge_rows, adjacency_tiles, picker):
    latent = node_blocks.shape[-1]
    blocks = node_blocks.shape[0]
    block_rows = node_blocks.shape[1]
    degree = picker.shape[0] // blocks
    extended = jnp.concatenate([node_blocks, received], axis=0)
    sources = jnp.einsum(
        "sn,nbd->sbd", picker, extended, preferred_element_type=jnp.float32
    ).astype(jnp.bfloat16)
    mixed_rows = jnp.einsum(
        "sij,sjd->sid", adjacency_tiles, sources, preferred_element_type=jnp.float32
    ).astype(jnp.bfloat16)
    self_term = jnp.dot(
        node_blocks.reshape(-1, latent),
        w_edge_in[latent : 2 * latent],
        preferred_element_type=jnp.float32,
    )
    pre_edge = jnp.dot(edge_rows, w_edge_in[:latent], preferred_element_type=jnp.float32) + jnp.dot(
        mixed_rows.reshape(-1, latent), w_edge_in[2 * latent :], preferred_element_type=jnp.float32
    )
    pre_edge = (
        pre_edge.reshape(blocks, degree, block_rows, latent)
        + self_term.reshape(blocks, 1, block_rows, latent)
    ).reshape(-1, latent)
    edge_hidden = jax.nn.silu(pre_edge).astype(jnp.bfloat16)
    return layer_norm(jnp.dot(edge_hidden, w_edge_out, preferred_element_type=jnp.float32))


def node_part(node_blocks, messages, w_node_in, w_node_out, edge_rows, live_weight):
    latent = node_blocks.shape[-1]
    blocks = node_blocks.shape[0]
    block_rows = node_blocks.shape[1]
    edges_out = (edge_rows.astype(jnp.float32) + messages).astype(jnp.bfloat16)
    gathered = jnp.sum(
        messages.reshape(blocks, -1, block_rows, latent) * live_weight[:, :, None, None], axis=1
    ).astype(jnp.bfloat16)
    flat_nodes = node_blocks.reshape(-1, latent)
    pre_node = jnp.dot(
        flat_nodes, w_node_in[:latent], preferred_element_type=jnp.float32
    ) + jnp.dot(
        gathered.reshape(-1, latent), w_node_in[latent:], preferred_element_type=jnp.float32
    )
    node_hidden = jax.nn.silu(pre_node).astype(jnp.bfloat16)
    nodes_out = (
        flat_nodes.astype(jnp.float32)
        + layer_norm(jnp.dot(node_hidden, w_node_out, preferred_element_type=jnp.float32))
    ).astype(jnp.bfloat16)
    return (nodes_out, edges_out)


def across_rows(face_rows, offset):
    return passed_along(face_rows, "gx", offset)


def across_cols(face_rows, offset):
    return passed_along(face_rows, "gy", offset)


def across_segment(face_rows, offset):
    return passed_along(face_rows, "segment", offset)


def swap_faces(face_blocks):
    return jnp.stack(
        [
            across_rows(face_blocks[1], 1),
            across_rows(face_blocks[0], -1),
            across_cols(face_blocks[3], 1),
            across_cols(face_blocks[2], -1),
            across_segment(face_blocks[5], 1),
            across_segment(face_blocks[4], -1),
        ],
        axis=0,
    )


def shards(
    node_latent,
    edge_latent,
    adjacency,
    neighbours,
    live,
    send_blocks,
    w_edge_in,
    w_edge_out,
    w_node_in,
    w_node_out,
    node_cotangent,
    edge_cotangent,
):
    latent = node_latent.shape[1]
    blocks, degree = neighbours.shape
    block_rows = adjacency.shape[-1]
    node_blocks = node_latent.reshape(blocks, block_rows, latent)
    choose = (send_blocks[0][:, None] == jnp.arange(blocks, dtype=jnp.int32)[None, :]).astype(
        jnp.bfloat16
    )
    outgoing = jnp.einsum(
        "jn,nbd->jbd", choose, node_blocks, preferred_element_type=jnp.float32
    ).astype(jnp.bfloat16)
    received = swap_faces(outgoing)
    adjacency_tiles = adjacency.reshape(blocks * degree, block_rows, block_rows)
    picker = (
        neighbours.reshape(-1)[:, None] == jnp.arange(blocks + 6, dtype=jnp.int32)[None, :]
    ).astype(jnp.bfloat16)
    live_weight = live.astype(jnp.float32)
    messages, edge_pull = jax.vjp(
        partial(edge_part, edge_rows=edge_latent, adjacency_tiles=adjacency_tiles, picker=picker),
        node_blocks,
        received,
        w_edge_in,
        w_edge_out,
    )
    outputs, node_pull = jax.vjp(
        partial(node_part, edge_rows=edge_latent, live_weight=live_weight),
        node_blocks,
        messages,
        w_node_in,
        w_node_out,
    )
    node_direct, message_ct, grad_ni, grad_no = node_pull((node_cotangent, edge_cotangent))
    node_terms = (grad_ni.astype(jnp.float32).reshape(-1), grad_no.astype(jnp.float32).reshape(-1))
    node_indirect, received_ct, grad_ei, grad_eo = edge_pull(message_ct)
    returned = swap_faces(received_ct)
    node_grad = node_direct.astype(jnp.float32) + node_indirect.astype(jnp.float32)
    node_grad = node_grad + jnp.einsum(
        "jn,jbd->nbd", choose, returned, preferred_element_type=jnp.float32
    )
    edge_terms = (grad_ei.astype(jnp.float32).reshape(-1), grad_eo.astype(jnp.float32).reshape(-1))
    devices = 1 << len(INDEX_BITS)
    edge_share = halving_scatter(
        jnp.concatenate([term.reshape(devices, -1) for term in edge_terms], axis=1), EDGE_ORDER
    )
    node_share = halving_scatter(
        jnp.concatenate([term.reshape(devices, -1) for term in node_terms], axis=1), NODE_ORDER
    )
    edge_cut = edge_terms[0].shape[0] // devices
    node_cut = node_terms[0].shape[0] // devices
    shares = (
        edge_share[:edge_cut],
        edge_share[edge_cut:],
        node_share[:node_cut],
        node_share[node_cut:],
    )
    return (
        outputs[0],
        outputs[1],
        node_grad.reshape(-1, latent),
        shares[0],
        shares[1],
        shares[2],
        shares[3],
    )


def solution(mesh):
    placed = (
        P(("segment", "gx", "gy"), None),
        P(("segment", "gx", "gy"), None),
        P(("segment", "gx", "gy"), None, None, None),
        P(("segment", "gx", "gy"), None),
        P(("segment", "gx", "gy"), None),
        P(("segment", "gx", "gy"), None),
        P(),
        P(),
        P(),
        P(),
        P(("segment", "gx", "gy"), None),
        P(("segment", "gx", "gy"), None),
    )
    return jax.shard_map(
        shards,
        mesh=mesh,
        in_specs=placed,
        out_specs=(
            P(("segment", "gx", "gy"), None),
            P(("segment", "gx", "gy"), None),
            P(("segment", "gx", "gy"), None),
            P(("segment", "gx", "gy")),
            P(("segment", "gx", "gy")),
            P(("segment", "gx", "gy")),
            P(("segment", "gx", "gy")),
        ),
        check_vma=False,
    )
```

```python
from functools import partial

import jax
import jax.numpy as jnp
from jax import lax
from jax.sharding import PartitionSpec as P


def passed_along(block, axis, distance):
    devices = range(lax.axis_size(axis))
    route = [(i - distance, i) for i in devices if i - distance in devices]
    return lax.ppermute(block, axis, route)


INDEX_BITS = (("segment", 0), ("gx", 2), ("gx", 1), ("gx", 0), ("gy", 3), ("gy", 2), ("gy", 1), ("gy", 0))
EDGE_ORDER = (7, 0, 6, 2, 5, 3, 1, 4)
NODE_ORDER = (7, 6, 2, 0, 3, 5, 4, 1)

def halving_scatter(rows, order):
    bits = len(INDEX_BITS)
    parts = rows.reshape((2,) * bits + rows.shape[1:]).transpose(tuple(order) + (bits,))
    for position in order:
        axis, bit = INDEX_BITS[position]
        side = (lax.axis_index(axis) >> bit) & 1
        route = [(j, j ^ (1 << bit)) for j in range(lax.axis_size(axis))]
        keep = lax.dynamic_index_in_dim(parts, side, 0, keepdims=False)
        send = lax.dynamic_index_in_dim(parts, 1 - side, 0, keepdims=False)
        if axis == "gy" and bit == 0:
            parts = keep + lax.ppermute(send, axis, route)
        else:
            arrived = lax.ppermute(send.astype(jnp.bfloat16), axis, route)
            parts = keep + arrived.astype(jnp.float32)
    return parts


def layer_norm(values):
    average = jnp.mean(values, axis=-1, keepdims=True)
    centred = values - average
    return centred * lax.rsqrt(jnp.mean(centred * centred, axis=-1, keepdims=True) + 1e-05)


def edge_part(node_blocks, received, w_edge_in, w_edge_out, edge_rows, adjacency_tiles, picker):
    latent = node_blocks.shape[-1]
    blocks = node_blocks.shape[0]
    block_rows = node_blocks.shape[1]
    degree = picker.shape[0] // blocks
    extended = jnp.concatenate([node_blocks, received], axis=0)
    sources = (
        jnp.dot(picker, extended.reshape(extended.shape[0], -1), preferred_element_type=jnp.float32)
        .astype(jnp.bfloat16)
        .reshape(picker.shape[0], block_rows, latent)
    )
    mixed_rows = jnp.einsum(
        "sij,sjd->sid", adjacency_tiles, sources, preferred_element_type=jnp.float32
    ).astype(jnp.bfloat16)
    self_term = jnp.dot(
        node_blocks.reshape(-1, latent),
        w_edge_in[latent : 2 * latent],
        preferred_element_type=jnp.float32,
    )
    pre_edge = jnp.dot(edge_rows, w_edge_in[:latent], preferred_element_type=jnp.float32) + jnp.dot(
        mixed_rows.reshape(-1, latent), w_edge_in[2 * latent :], preferred_element_type=jnp.float32
    )
    pre_edge = (
        pre_edge.reshape(blocks, degree, block_rows, latent)
        + self_term.reshape(blocks, 1, block_rows, latent)
    ).reshape(-1, latent)
    edge_hidden = jax.nn.silu(pre_edge).astype(jnp.bfloat16)
    return layer_norm(jnp.dot(edge_hidden, w_edge_out, preferred_element_type=jnp.float32))


def node_part(node_blocks, messages, w_node_in, w_node_out, edge_rows, live_weight):
    latent = node_blocks.shape[-1]
    blocks = node_blocks.shape[0]
    block_rows = node_blocks.shape[1]
    edges_out = (edge_rows.astype(jnp.float32) + messages).astype(jnp.bfloat16)
    gathered = jnp.sum(
        messages.reshape(blocks, -1, block_rows, latent) * live_weight[:, :, None, None], axis=1
    ).astype(jnp.bfloat16)
    flat_nodes = node_blocks.reshape(-1, latent)
    pre_node = jnp.dot(
        flat_nodes, w_node_in[:latent], preferred_element_type=jnp.float32
    ) + jnp.dot(
        gathered.reshape(-1, latent), w_node_in[latent:], preferred_element_type=jnp.float32
    )
    node_hidden = jax.nn.silu(pre_node).astype(jnp.bfloat16)
    nodes_out = (
        flat_nodes.astype(jnp.float32)
        + layer_norm(jnp.dot(node_hidden, w_node_out, preferred_element_type=jnp.float32))
    ).astype(jnp.bfloat16)
    return (nodes_out, edges_out)


def across_rows(face_rows, offset):
    return passed_along(face_rows, "gx", offset)


def across_cols(face_rows, offset):
    return passed_along(face_rows, "gy", offset)


def across_segment(face_rows, offset):
    return passed_along(face_rows, "segment", offset)


def swap_faces(face_blocks):
    return jnp.stack(
        [
            across_rows(face_blocks[1], 1),
            across_rows(face_blocks[0], -1),
            across_cols(face_blocks[3], 1),
            across_cols(face_blocks[2], -1),
            across_segment(face_blocks[5], 1),
            across_segment(face_blocks[4], -1),
        ],
        axis=0,
    )


def shards(
    node_latent,
    edge_latent,
    adjacency,
    neighbours,
    live,
    send_blocks,
    w_edge_in,
    w_edge_out,
    w_node_in,
    w_node_out,
    node_cotangent,
    edge_cotangent,
):
    latent = node_latent.shape[1]
    blocks, degree = neighbours.shape
    block_rows = adjacency.shape[-1]
    node_blocks = node_latent.reshape(blocks, block_rows, latent)
    choose = (send_blocks[0][:, None] == jnp.arange(blocks, dtype=jnp.int32)[None, :]).astype(
        jnp.bfloat16
    )
    outgoing = (
        jnp.dot(choose, node_blocks.reshape(blocks, -1), preferred_element_type=jnp.float32)
        .astype(jnp.bfloat16)
        .reshape(choose.shape[0], block_rows, latent)
    )
    received = swap_faces(outgoing)
    adjacency_tiles = adjacency.reshape(blocks * degree, block_rows, block_rows)
    picker = (
        neighbours.reshape(-1)[:, None] == jnp.arange(blocks + 6, dtype=jnp.int32)[None, :]
    ).astype(jnp.bfloat16)
    live_weight = live.astype(jnp.float32)
    messages, edge_pull = jax.vjp(
        partial(edge_part, edge_rows=edge_latent, adjacency_tiles=adjacency_tiles, picker=picker),
        node_blocks,
        received,
        w_edge_in,
        w_edge_out,
    )
    outputs, node_pull = jax.vjp(
        partial(node_part, edge_rows=edge_latent, live_weight=live_weight),
        node_blocks,
        messages,
        w_node_in,
        w_node_out,
    )
    node_direct, message_ct, grad_ni, grad_no = node_pull((node_cotangent, edge_cotangent))
    node_terms = (grad_ni.astype(jnp.float32).reshape(-1), grad_no.astype(jnp.float32).reshape(-1))
    node_indirect, received_ct, grad_ei, grad_eo = edge_pull(message_ct)
    returned = swap_faces(received_ct)
    node_grad = node_direct.astype(jnp.float32) + node_indirect.astype(jnp.float32)
    node_grad = node_grad + jnp.dot(
        choose.T, returned.reshape(returned.shape[0], -1), preferred_element_type=jnp.float32
    ).reshape(blocks, block_rows, latent)
    edge_terms = (grad_ei.astype(jnp.float32).reshape(-1), grad_eo.astype(jnp.float32).reshape(-1))
    devices = 1 << len(INDEX_BITS)
    edge_share = halving_scatter(
        jnp.concatenate([term.reshape(devices, -1) for term in edge_terms], axis=1), EDGE_ORDER
    )
    node_share = halving_scatter(
        jnp.concatenate([term.reshape(devices, -1) for term in node_terms], axis=1), NODE_ORDER
    )
    edge_cut = edge_terms[0].shape[0] // devices
    node_cut = node_terms[0].shape[0] // devices
    shares = (
        edge_share[:edge_cut],
        edge_share[edge_cut:],
        node_share[:node_cut],
        node_share[node_cut:],
    )
    return (
        outputs[0],
        outputs[1],
        node_grad.reshape(-1, latent),
        shares[0],
        shares[1],
        shares[2],
        shares[3],
    )


def solution(mesh):
    placed = (
        P(("segment", "gx", "gy"), None),
        P(("segment", "gx", "gy"), None),
        P(("segment", "gx", "gy"), None, None, None),
        P(("segment", "gx", "gy"), None),
        P(("segment", "gx", "gy"), None),
        P(("segment", "gx", "gy"), None),
        P(),
        P(),
        P(),
        P(),
        P(("segment", "gx", "gy"), None),
        P(("segment", "gx", "gy"), None),
    )
    return jax.shard_map(
        shards,
        mesh=mesh,
        in_specs=placed,
        out_specs=(
            P(("segment", "gx", "gy"), None),
            P(("segment", "gx", "gy"), None),
            P(("segment", "gx", "gy"), None),
            P(("segment", "gx", "gy")),
            P(("segment", "gx", "gy")),
            P(("segment", "gx", "gy")),
            P(("segment", "gx", "gy")),
        ),
        check_vma=False,
    )
```

```python
from functools import partial

import jax
import jax.numpy as jnp
from jax import lax
from jax.sharding import PartitionSpec as P


def passed_along(block, axis, distance):
    devices = range(lax.axis_size(axis))
    route = [(i - distance, i) for i in devices if i - distance in devices]
    return lax.ppermute(block, axis, route)


INDEX_BITS = (("segment", 0), ("gx", 2), ("gx", 1), ("gx", 0), ("gy", 3), ("gy", 2), ("gy", 1), ("gy", 0))
EDGE_ORDER = (7, 0, 6, 2, 5, 3, 1, 4)
NODE_ORDER = (7, 6, 2, 0, 3, 5, 4, 1)

def halving_scatter(rows, order):
    bits = len(INDEX_BITS)
    parts = rows.reshape((2,) * bits + rows.shape[1:]).transpose(tuple(order) + (bits,))
    for position in order:
        axis, bit = INDEX_BITS[position]
        side = (lax.axis_index(axis) >> bit) & 1
        route = [(j, j ^ (1 << bit)) for j in range(lax.axis_size(axis))]
        keep = lax.dynamic_index_in_dim(parts, side, 0, keepdims=False)
        send = lax.dynamic_index_in_dim(parts, 1 - side, 0, keepdims=False)
        if axis == "gy" and bit == 0:
            parts = keep + lax.ppermute(send, axis, route)
        else:
            arrived = lax.ppermute(send.astype(jnp.bfloat16), axis, route)
            parts = keep + arrived.astype(jnp.float32)
    return parts


def layer_norm(values):
    average = jnp.mean(values, axis=-1, keepdims=True)
    centred = values - average
    return centred * lax.rsqrt(jnp.mean(centred * centred, axis=-1, keepdims=True) + 1e-05)


def edge_part(node_blocks, received, w_edge_in, w_edge_out, edge_rows, adjacency_tiles, picker):
    latent = node_blocks.shape[-1]
    blocks = node_blocks.shape[0]
    block_rows = node_blocks.shape[1]
    degree = picker.shape[0] // blocks
    extended = jnp.concatenate([node_blocks] + [block[None] for block in received], axis=0)
    sources = jnp.einsum(
        "sn,nbd->sbd", picker, extended, preferred_element_type=jnp.float32
    ).astype(jnp.bfloat16)
    mixed_rows = jnp.einsum(
        "sij,sjd->sid", adjacency_tiles, sources, preferred_element_type=jnp.float32
    ).astype(jnp.bfloat16)
    self_term = jnp.dot(
        node_blocks.reshape(-1, latent),
        w_edge_in[latent : 2 * latent],
        preferred_element_type=jnp.float32,
    )
    pre_edge = jnp.dot(edge_rows, w_edge_in[:latent], preferred_element_type=jnp.float32) + jnp.dot(
        mixed_rows.reshape(-1, latent), w_edge_in[2 * latent :], preferred_element_type=jnp.float32
    )
    pre_edge = (
        pre_edge.reshape(blocks, degree, block_rows, latent)
        + self_term.reshape(blocks, 1, block_rows, latent)
    ).reshape(-1, latent)
    edge_hidden = jax.nn.silu(pre_edge).astype(jnp.bfloat16)
    return layer_norm(jnp.dot(edge_hidden, w_edge_out, preferred_element_type=jnp.float32))


def node_part(node_blocks, messages, w_node_in, w_node_out, edge_rows, live_weight):
    latent = node_blocks.shape[-1]
    blocks = node_blocks.shape[0]
    block_rows = node_blocks.shape[1]
    edges_out = (edge_rows.astype(jnp.float32) + messages).astype(jnp.bfloat16)
    gathered = jnp.sum(
        messages.reshape(blocks, -1, block_rows, latent) * live_weight[:, :, None, None], axis=1
    ).astype(jnp.bfloat16)
    flat_nodes = node_blocks.reshape(-1, latent)
    pre_node = jnp.dot(
        flat_nodes, w_node_in[:latent], preferred_element_type=jnp.float32
    ) + jnp.dot(
        gathered.reshape(-1, latent), w_node_in[latent:], preferred_element_type=jnp.float32
    )
    node_hidden = jax.nn.silu(pre_node).astype(jnp.bfloat16)
    nodes_out = (
        flat_nodes.astype(jnp.float32)
        + layer_norm(jnp.dot(node_hidden, w_node_out, preferred_element_type=jnp.float32))
    ).astype(jnp.bfloat16)
    return (nodes_out, edges_out)


def across_rows(face_rows, offset):
    return passed_along(face_rows, "gx", offset)


def across_cols(face_rows, offset):
    return passed_along(face_rows, "gy", offset)


def across_segment(face_rows, offset):
    return passed_along(face_rows, "segment", offset)


def swap_faces(face_blocks):
    return [
        across_rows(face_blocks[1], 1),
        across_rows(face_blocks[0], -1),
        across_cols(face_blocks[3], 1),
        across_cols(face_blocks[2], -1),
        across_segment(face_blocks[5], 1),
        across_segment(face_blocks[4], -1),
    ]


def shards(
    node_latent,
    edge_latent,
    adjacency,
    neighbours,
    live,
    send_blocks,
    w_edge_in,
    w_edge_out,
    w_node_in,
    w_node_out,
    node_cotangent,
    edge_cotangent,
):
    latent = node_latent.shape[1]
    blocks, degree = neighbours.shape
    block_rows = adjacency.shape[-1]
    node_blocks = node_latent.reshape(blocks, block_rows, latent)
    choose = (send_blocks[0][:, None] == jnp.arange(blocks, dtype=jnp.int32)[None, :]).astype(
        jnp.bfloat16
    )
    outgoing = jnp.einsum(
        "jn,nbd->jbd", choose, node_blocks, preferred_element_type=jnp.float32
    ).astype(jnp.bfloat16)
    received = swap_faces(outgoing)
    adjacency_tiles = adjacency.reshape(blocks * degree, block_rows, block_rows)
    picker = (
        neighbours.reshape(-1)[:, None] == jnp.arange(blocks + 6, dtype=jnp.int32)[None, :]
    ).astype(jnp.bfloat16)
    live_weight = live.astype(jnp.float32)
    messages, edge_pull = jax.vjp(
        partial(edge_part, edge_rows=edge_latent, adjacency_tiles=adjacency_tiles, picker=picker),
        node_blocks,
        received,
        w_edge_in,
        w_edge_out,
    )
    outputs, node_pull = jax.vjp(
        partial(node_part, edge_rows=edge_latent, live_weight=live_weight),
        node_blocks,
        messages,
        w_node_in,
        w_node_out,
    )
    node_direct, message_ct, grad_ni, grad_no = node_pull((node_cotangent, edge_cotangent))
    node_terms = (grad_ni.astype(jnp.float32).reshape(-1), grad_no.astype(jnp.float32).reshape(-1))
    node_indirect, received_ct, grad_ei, grad_eo = edge_pull(message_ct)
    returned = swap_faces(received_ct)
    node_grad = node_direct.astype(jnp.float32) + node_indirect.astype(jnp.float32)
    for face, block in enumerate(returned):
        node_grad = node_grad + choose[face].astype(jnp.float32)[:, None, None] * block.astype(
            jnp.float32
        )
    edge_terms = (grad_ei.astype(jnp.float32).reshape(-1), grad_eo.astype(jnp.float32).reshape(-1))
    devices = 1 << len(INDEX_BITS)
    edge_share = halving_scatter(
        jnp.concatenate([term.reshape(devices, -1) for term in edge_terms], axis=1), EDGE_ORDER
    )
    node_share = halving_scatter(
        jnp.concatenate([term.reshape(devices, -1) for term in node_terms], axis=1), NODE_ORDER
    )
    edge_cut = edge_terms[0].shape[0] // devices
    node_cut = node_terms[0].shape[0] // devices
    shares = (
        edge_share[:edge_cut],
        edge_share[edge_cut:],
        node_share[:node_cut],
        node_share[node_cut:],
    )
    return (
        outputs[0],
        outputs[1],
        node_grad.reshape(-1, latent),
        shares[0],
        shares[1],
        shares[2],
        shares[3],
    )


def solution(mesh):
    placed = (
        P(("segment", "gx", "gy"), None),
        P(("segment", "gx", "gy"), None),
        P(("segment", "gx", "gy"), None, None, None),
        P(("segment", "gx", "gy"), None),
        P(("segment", "gx", "gy"), None),
        P(("segment", "gx", "gy"), None),
        P(),
        P(),
        P(),
        P(),
        P(("segment", "gx", "gy"), None),
        P(("segment", "gx", "gy"), None),
    )
    return jax.shard_map(
        shards,
        mesh=mesh,
        in_specs=placed,
        out_specs=(
            P(("segment", "gx", "gy"), None),
            P(("segment", "gx", "gy"), None),
            P(("segment", "gx", "gy"), None),
            P(("segment", "gx", "gy")),
            P(("segment", "gx", "gy")),
            P(("segment", "gx", "gy")),
            P(("segment", "gx", "gy")),
        ),
        check_vma=False,
    )
```

```python
from functools import partial

import jax
import jax.numpy as jnp
from jax import lax
from jax.sharding import PartitionSpec as P


def passed_along(block, axis, distance):
    devices = range(lax.axis_size(axis))
    route = [(i - distance, i) for i in devices if i - distance in devices]
    return lax.ppermute(block, axis, route)


INDEX_BITS = (("segment", 0), ("gx", 2), ("gx", 1), ("gx", 0), ("gy", 3), ("gy", 2), ("gy", 1), ("gy", 0))
EDGE_ORDER = (7, 0, 6, 2, 5, 3, 1, 4)
NODE_ORDER = (7, 6, 2, 0, 3, 5, 4, 1)

def halving_scatter(rows, order):
    bits = len(INDEX_BITS)
    parts = rows.reshape((2,) * bits + rows.shape[1:]).transpose(tuple(order) + (bits,))
    for position in order:
        axis, bit = INDEX_BITS[position]
        side = (lax.axis_index(axis) >> bit) & 1
        route = [(j, j ^ (1 << bit)) for j in range(lax.axis_size(axis))]
        keep = lax.dynamic_index_in_dim(parts, side, 0, keepdims=False)
        send = lax.dynamic_index_in_dim(parts, 1 - side, 0, keepdims=False)
        arrived = lax.ppermute(send.astype(jnp.bfloat16), axis, route)
        parts = keep + arrived.astype(jnp.float32)
    return parts


def layer_norm(values):
    average = jnp.mean(values, axis=-1, keepdims=True)
    centred = values - average
    return centred * lax.rsqrt(jnp.mean(centred * centred, axis=-1, keepdims=True) + 1e-05)


def edge_part(node_blocks, received, w_edge_in, w_edge_out, edge_rows, adjacency_tiles, picker):
    latent = node_blocks.shape[-1]
    blocks = node_blocks.shape[0]
    block_rows = node_blocks.shape[1]
    degree = picker.shape[0] // blocks
    extended = jnp.concatenate([node_blocks] + [block[None] for block in received], axis=0)
    sources = jnp.einsum(
        "sn,nbd->sbd", picker, extended, preferred_element_type=jnp.float32
    ).astype(jnp.bfloat16)
    mixed_rows = jnp.einsum(
        "sij,sjd->sid", adjacency_tiles, sources, preferred_element_type=jnp.float32
    ).astype(jnp.bfloat16)
    self_term = jnp.dot(
        node_blocks.reshape(-1, latent),
        w_edge_in[latent : 2 * latent],
        preferred_element_type=jnp.float32,
    )
    pre_edge = jnp.dot(edge_rows, w_edge_in[:latent], preferred_element_type=jnp.float32) + jnp.dot(
        mixed_rows.reshape(-1, latent), w_edge_in[2 * latent :], preferred_element_type=jnp.float32
    )
    pre_edge = (
        pre_edge.reshape(blocks, degree, block_rows, latent)
        + self_term.reshape(blocks, 1, block_rows, latent)
    ).reshape(-1, latent)
    edge_hidden = jax.nn.silu(pre_edge).astype(jnp.bfloat16)
    return layer_norm(jnp.dot(edge_hidden, w_edge_out, preferred_element_type=jnp.float32))


def node_part(node_blocks, messages, w_node_in, w_node_out, edge_rows, live_weight):
    latent = node_blocks.shape[-1]
    blocks = node_blocks.shape[0]
    block_rows = node_blocks.shape[1]
    edges_out = (edge_rows.astype(jnp.float32) + messages).astype(jnp.bfloat16)
    gathered = jnp.sum(
        messages.reshape(blocks, -1, block_rows, latent) * live_weight[:, :, None, None], axis=1
    ).astype(jnp.bfloat16)
    flat_nodes = node_blocks.reshape(-1, latent)
    pre_node = jnp.dot(
        flat_nodes, w_node_in[:latent], preferred_element_type=jnp.float32
    ) + jnp.dot(
        gathered.reshape(-1, latent), w_node_in[latent:], preferred_element_type=jnp.float32
    )
    node_hidden = jax.nn.silu(pre_node).astype(jnp.bfloat16)
    nodes_out = (
        flat_nodes.astype(jnp.float32)
        + layer_norm(jnp.dot(node_hidden, w_node_out, preferred_element_type=jnp.float32))
    ).astype(jnp.bfloat16)
    return (nodes_out, edges_out)


def across_rows(face_rows, offset):
    return passed_along(face_rows, "gx", offset)


def across_cols(face_rows, offset):
    return passed_along(face_rows, "gy", offset)


def across_segment(face_rows, offset):
    return passed_along(face_rows, "segment", offset)


def swap_faces(face_blocks):
    return [
        across_rows(face_blocks[1], 1),
        across_rows(face_blocks[0], -1),
        across_cols(face_blocks[3], 1),
        across_cols(face_blocks[2], -1),
        across_segment(face_blocks[5], 1),
        across_segment(face_blocks[4], -1),
    ]


def shards(
    node_latent,
    edge_latent,
    adjacency,
    neighbours,
    live,
    send_blocks,
    w_edge_in,
    w_edge_out,
    w_node_in,
    w_node_out,
    node_cotangent,
    edge_cotangent,
):
    latent = node_latent.shape[1]
    blocks, degree = neighbours.shape
    block_rows = adjacency.shape[-1]
    node_blocks = node_latent.reshape(blocks, block_rows, latent)
    choose = (send_blocks[0][:, None] == jnp.arange(blocks, dtype=jnp.int32)[None, :]).astype(
        jnp.bfloat16
    )
    outgoing = jnp.einsum(
        "jn,nbd->jbd", choose, node_blocks, preferred_element_type=jnp.float32
    ).astype(jnp.bfloat16)
    received = swap_faces(outgoing)
    adjacency_tiles = adjacency.reshape(blocks * degree, block_rows, block_rows)
    picker = (
        neighbours.reshape(-1)[:, None] == jnp.arange(blocks + 6, dtype=jnp.int32)[None, :]
    ).astype(jnp.bfloat16)
    live_weight = live.astype(jnp.float32)
    messages, edge_pull = jax.vjp(
        partial(edge_part, edge_rows=edge_latent, adjacency_tiles=adjacency_tiles, picker=picker),
        node_blocks,
        received,
        w_edge_in,
        w_edge_out,
    )
    outputs, node_pull = jax.vjp(
        partial(node_part, edge_rows=edge_latent, live_weight=live_weight),
        node_blocks,
        messages,
        w_node_in,
        w_node_out,
    )
    node_direct, message_ct, grad_ni, grad_no = node_pull((node_cotangent, edge_cotangent))
    node_terms = (grad_ni.astype(jnp.float32).reshape(-1), grad_no.astype(jnp.float32).reshape(-1))
    node_indirect, received_ct, grad_ei, grad_eo = edge_pull(message_ct)
    returned = swap_faces(received_ct)
    node_grad = node_direct.astype(jnp.float32) + node_indirect.astype(jnp.float32)
    for face, block in enumerate(returned):
        node_grad = node_grad + choose[face].astype(jnp.float32)[:, None, None] * block.astype(
            jnp.float32
        )
    edge_terms = (grad_ei.astype(jnp.float32).reshape(-1), grad_eo.astype(jnp.float32).reshape(-1))
    devices = 1 << len(INDEX_BITS)
    edge_share = halving_scatter(
        jnp.concatenate([term.reshape(devices, -1) for term in edge_terms], axis=1), EDGE_ORDER
    )
    node_share = halving_scatter(
        jnp.concatenate([term.reshape(devices, -1) for term in node_terms], axis=1), NODE_ORDER
    )
    edge_cut = edge_terms[0].shape[0] // devices
    node_cut = node_terms[0].shape[0] // devices
    shares = (
        edge_share[:edge_cut],
        edge_share[edge_cut:],
        node_share[:node_cut],
        node_share[node_cut:],
    )
    return (
        outputs[0],
        outputs[1],
        node_grad.reshape(-1, latent),
        shares[0],
        shares[1],
        shares[2],
        shares[3],
    )


def solution(mesh):
    placed = (
        P(("segment", "gx", "gy"), None),
        P(("segment", "gx", "gy"), None),
        P(("segment", "gx", "gy"), None, None, None),
        P(("segment", "gx", "gy"), None),
        P(("segment", "gx", "gy"), None),
        P(("segment", "gx", "gy"), None),
        P(),
        P(),
        P(),
        P(),
        P(("segment", "gx", "gy"), None),
        P(("segment", "gx", "gy"), None),
    )
    return jax.shard_map(
        shards,
        mesh=mesh,
        in_specs=placed,
        out_specs=(
            P(("segment", "gx", "gy"), None),
            P(("segment", "gx", "gy"), None),
            P(("segment", "gx", "gy"), None),
            P(("segment", "gx", "gy")),
            P(("segment", "gx", "gy")),
            P(("segment", "gx", "gy")),
            P(("segment", "gx", "gy")),
        ),
        check_vma=False,
    )
```

```python
from functools import partial

import jax
import jax.numpy as jnp
from jax import lax
from jax.sharding import PartitionSpec as P


def passed_along(block, axis, distance):
    devices = range(lax.axis_size(axis))
    route = [(i - distance, i) for i in devices if i - distance in devices]
    return lax.ppermute(block, axis, route)


INDEX_BITS = (("segment", 0), ("gx", 2), ("gx", 1), ("gx", 0), ("gy", 3), ("gy", 2), ("gy", 1), ("gy", 0))
EDGE_ORDER = (7, 0, 6, 2, 5, 3, 1, 4)
NODE_ORDER = (7, 6, 2, 0, 3, 5, 4, 1)

def halving_scatter(rows, order):
    bits = len(INDEX_BITS)
    parts = rows.reshape((2,) * bits + rows.shape[1:]).transpose(tuple(order) + (bits,))
    for position in order:
        axis, bit = INDEX_BITS[position]
        side = (lax.axis_index(axis) >> bit) & 1
        route = [(j, j ^ (1 << bit)) for j in range(lax.axis_size(axis))]
        keep = lax.dynamic_index_in_dim(parts, side, 0, keepdims=False)
        send = lax.dynamic_index_in_dim(parts, 1 - side, 0, keepdims=False)
        arrived = lax.ppermute(send.astype(jnp.bfloat16), axis, route)
        parts = keep + arrived.astype(jnp.float32)
    return parts


def layer_norm(values):
    average = jnp.mean(values, axis=-1, keepdims=True)
    centred = values - average
    return centred * lax.rsqrt(jnp.mean(centred * centred, axis=-1, keepdims=True) + 1e-05)


def edge_part(node_blocks, received, w_edge_in, w_edge_out, edge_rows, adjacency_tiles, picker):
    latent = node_blocks.shape[-1]
    blocks = node_blocks.shape[0]
    block_rows = node_blocks.shape[1]
    degree = picker.shape[0] // blocks
    extended = jnp.concatenate([node_blocks] + [block[None] for block in received], axis=0)
    sources = jnp.einsum(
        "sn,nbd->sbd", picker, extended, preferred_element_type=jnp.float32
    ).astype(jnp.bfloat16)
    mixed_rows = jnp.einsum(
        "sij,sjd->sid", adjacency_tiles, sources, preferred_element_type=jnp.float32
    ).astype(jnp.bfloat16)
    self_term = jnp.dot(
        node_blocks.reshape(-1, latent),
        w_edge_in[latent : 2 * latent],
        preferred_element_type=jnp.float32,
    )
    pre_edge = jnp.dot(edge_rows, w_edge_in[:latent], preferred_element_type=jnp.float32) + jnp.dot(
        mixed_rows.reshape(-1, latent), w_edge_in[2 * latent :], preferred_element_type=jnp.float32
    )
    pre_edge = (
        pre_edge.reshape(blocks, degree, block_rows, latent)
        + self_term.reshape(blocks, 1, block_rows, latent)
    ).reshape(-1, latent)
    edge_hidden = jax.nn.silu(pre_edge).astype(jnp.bfloat16)
    return layer_norm(jnp.dot(edge_hidden, w_edge_out, preferred_element_type=jnp.float32))


def node_part(node_blocks, messages, w_node_in, w_node_out, edge_rows, live_weight):
    latent = node_blocks.shape[-1]
    blocks = node_blocks.shape[0]
    block_rows = node_blocks.shape[1]
    edges_out = (edge_rows.astype(jnp.float32) + messages).astype(jnp.bfloat16)
    gathered = jnp.sum(
        messages.reshape(blocks, -1, block_rows, latent) * live_weight[:, :, None, None], axis=1
    ).astype(jnp.bfloat16)
    flat_nodes = node_blocks.reshape(-1, latent)
    pre_node = jnp.dot(
        flat_nodes, w_node_in[:latent], preferred_element_type=jnp.float32
    ) + jnp.dot(
        gathered.reshape(-1, latent), w_node_in[latent:], preferred_element_type=jnp.float32
    )
    node_hidden = jax.nn.silu(pre_node).astype(jnp.bfloat16)
    nodes_out = (
        flat_nodes.astype(jnp.float32)
        + layer_norm(jnp.dot(node_hidden, w_node_out, preferred_element_type=jnp.float32))
    ).astype(jnp.bfloat16)
    return (nodes_out, edges_out)


def across_rows(face_rows, offset):
    return passed_along(face_rows, "gx", offset)


def across_cols(face_rows, offset):
    return passed_along(face_rows, "gy", offset)


def across_segment(face_rows, offset):
    return passed_along(face_rows, "segment", offset)


def swap_faces(face_blocks):
    return [
        across_rows(face_blocks[1], 1),
        across_rows(face_blocks[0], -1),
        across_cols(face_blocks[3], 1),
        across_cols(face_blocks[2], -1),
        across_segment(face_blocks[5], 1),
        across_segment(face_blocks[4], -1),
    ]


def shards(
    node_latent,
    edge_latent,
    adjacency,
    neighbours,
    live,
    send_blocks,
    w_edge_in,
    w_edge_out,
    w_node_in,
    w_node_out,
    node_cotangent,
    edge_cotangent,
):
    latent = node_latent.shape[1]
    blocks, degree = neighbours.shape
    block_rows = adjacency.shape[-1]
    node_blocks = node_latent.reshape(blocks, block_rows, latent)
    choose = (send_blocks[0][:, None] == jnp.arange(blocks, dtype=jnp.int32)[None, :]).astype(
        jnp.bfloat16
    )
    outgoing = jnp.einsum(
        "jn,nbd->jbd", choose, node_blocks, preferred_element_type=jnp.float32
    ).astype(jnp.bfloat16)
    received = swap_faces(outgoing)
    adjacency_tiles = adjacency.reshape(blocks * degree, block_rows, block_rows)
    picker = (
        neighbours.reshape(-1)[:, None] == jnp.arange(blocks + 6, dtype=jnp.int32)[None, :]
    ).astype(jnp.bfloat16)
    live_weight = live.astype(jnp.float32)
    messages, edge_pull = jax.vjp(
        partial(edge_part, edge_rows=edge_latent, adjacency_tiles=adjacency_tiles, picker=picker),
        node_blocks,
        received,
        w_edge_in,
        w_edge_out,
    )
    outputs, node_pull = jax.vjp(
        partial(node_part, edge_rows=edge_latent, live_weight=live_weight),
        node_blocks,
        messages,
        w_node_in,
        w_node_out,
    )
    node_direct, message_ct, grad_ni, grad_no = node_pull((node_cotangent, edge_cotangent))
    node_terms = (grad_ni.astype(jnp.float32).reshape(-1), grad_no.astype(jnp.float32).reshape(-1))
    node_indirect, received_ct, grad_ei, grad_eo = edge_pull(message_ct)
    returned = swap_faces(received_ct)
    node_grad = node_direct.astype(jnp.float32) + node_indirect.astype(jnp.float32)
    for face, block in enumerate(returned):
        node_grad = node_grad + choose[face].astype(jnp.float32)[:, None, None] * block.astype(
            jnp.float32
        )
    edge_terms = (grad_ei.astype(jnp.float32).reshape(-1), grad_eo.astype(jnp.float32).reshape(-1))
    devices = 1 << len(INDEX_BITS)
    edge_share = halving_scatter(edge_terms[0].reshape(devices, -1), EDGE_ORDER)
    node_share = halving_scatter(
        jnp.concatenate([term.reshape(devices, -1) for term in (edge_terms[1],) + node_terms], axis=1),
        NODE_ORDER,
    )
    out_cut = edge_terms[1].shape[0] // devices
    node_cut = out_cut + node_terms[0].shape[0] // devices
    shares = (
        edge_share,
        node_share[:out_cut],
        node_share[out_cut:node_cut],
        node_share[node_cut:],
    )
    return (
        outputs[0],
        outputs[1],
        node_grad.reshape(-1, latent),
        shares[0],
        shares[1],
        shares[2],
        shares[3],
    )


def solution(mesh):
    placed = (
        P(("segment", "gx", "gy"), None),
        P(("segment", "gx", "gy"), None),
        P(("segment", "gx", "gy"), None, None, None),
        P(("segment", "gx", "gy"), None),
        P(("segment", "gx", "gy"), None),
        P(("segment", "gx", "gy"), None),
        P(),
        P(),
        P(),
        P(),
        P(("segment", "gx", "gy"), None),
        P(("segment", "gx", "gy"), None),
    )
    return jax.shard_map(
        shards,
        mesh=mesh,
        in_specs=placed,
        out_specs=(
            P(("segment", "gx", "gy"), None),
            P(("segment", "gx", "gy"), None),
            P(("segment", "gx", "gy"), None),
            P(("segment", "gx", "gy")),
            P(("segment", "gx", "gy")),
            P(("segment", "gx", "gy")),
            P(("segment", "gx", "gy")),
        ),
        check_vma=False,
    )
```

```python
from functools import partial

import jax
import jax.numpy as jnp
from jax import lax
from jax.sharding import PartitionSpec as P


def passed_along(block, axis, distance):
    devices = range(lax.axis_size(axis))
    route = [(i - distance, i) for i in devices if i - distance in devices]
    return lax.ppermute(block, axis, route)


INDEX_BITS = (("segment", 0), ("gx", 2), ("gx", 1), ("gx", 0), ("gy", 3), ("gy", 2), ("gy", 1), ("gy", 0))
EDGE_ORDER = (7, 0, 6, 2, 5, 3, 1, 4)
NODE_ORDER = (7, 6, 2, 0, 3, 5, 4, 1)

def halving_scatter(rows, order):
    bits = len(INDEX_BITS)
    parts = rows.reshape((2,) * bits + rows.shape[1:]).transpose(tuple(order) + (bits,))
    for position in order:
        axis, bit = INDEX_BITS[position]
        side = (lax.axis_index(axis) >> bit) & 1
        route = [(j, j ^ (1 << bit)) for j in range(lax.axis_size(axis))]
        keep = lax.dynamic_index_in_dim(parts, side, 0, keepdims=False)
        send = lax.dynamic_index_in_dim(parts, 1 - side, 0, keepdims=False)
        arrived = lax.ppermute(send.astype(jnp.bfloat16), axis, route)
        parts = keep + arrived.astype(jnp.float32)
    return parts


def layer_norm(values):
    average = jnp.mean(values, axis=-1, keepdims=True)
    centred = values - average
    return centred * lax.rsqrt(jnp.mean(centred * centred, axis=-1, keepdims=True) + 1e-05)


def edge_part(node_blocks, received, w_edge_in, w_edge_out, edge_rows, adjacency_tiles, picker):
    latent = node_blocks.shape[-1]
    blocks = node_blocks.shape[0]
    block_rows = node_blocks.shape[1]
    degree = picker.shape[0] // blocks
    extended = jnp.concatenate([node_blocks] + [block[None] for block in received], axis=0)
    sources = jnp.einsum(
        "sn,nbd->sbd", picker, extended, preferred_element_type=jnp.float32
    ).astype(jnp.bfloat16)
    mixed_rows = jnp.einsum(
        "sij,sjd->sid", adjacency_tiles, sources, preferred_element_type=jnp.float32
    ).astype(jnp.bfloat16)
    self_term = jnp.dot(
        node_blocks.reshape(-1, latent),
        w_edge_in[latent : 2 * latent],
        preferred_element_type=jnp.float32,
    )
    pre_edge = jnp.dot(edge_rows, w_edge_in[:latent], preferred_element_type=jnp.float32) + jnp.dot(
        mixed_rows.reshape(-1, latent), w_edge_in[2 * latent :], preferred_element_type=jnp.float32
    )
    pre_edge = (
        pre_edge.reshape(blocks, degree, block_rows, latent)
        + self_term.reshape(blocks, 1, block_rows, latent)
    ).reshape(-1, latent)
    edge_hidden = jax.nn.silu(pre_edge).astype(jnp.bfloat16)
    return layer_norm(jnp.dot(edge_hidden, w_edge_out, preferred_element_type=jnp.float32))


def node_part(node_blocks, messages, w_node_in, w_node_out, edge_rows, live_weight):
    latent = node_blocks.shape[-1]
    blocks = node_blocks.shape[0]
    block_rows = node_blocks.shape[1]
    edges_out = (edge_rows.astype(jnp.float32) + messages).astype(jnp.bfloat16)
    gathered = jnp.sum(
        messages.reshape(blocks, -1, block_rows, latent) * live_weight[:, :, None, None], axis=1
    ).astype(jnp.bfloat16)
    flat_nodes = node_blocks.reshape(-1, latent)
    pre_node = jnp.dot(
        flat_nodes, w_node_in[:latent], preferred_element_type=jnp.float32
    ) + jnp.dot(
        gathered.reshape(-1, latent), w_node_in[latent:], preferred_element_type=jnp.float32
    )
    node_hidden = jax.nn.silu(pre_node).astype(jnp.bfloat16)
    nodes_out = (
        flat_nodes.astype(jnp.float32)
        + layer_norm(jnp.dot(node_hidden, w_node_out, preferred_element_type=jnp.float32))
    ).astype(jnp.bfloat16)
    return (nodes_out, edges_out)


def across_rows(face_rows, offset):
    return passed_along(face_rows, "gx", offset)


def across_cols(face_rows, offset):
    return passed_along(face_rows, "gy", offset)


def across_segment(face_rows, offset):
    return passed_along(face_rows, "segment", offset)


def swap_faces(face_blocks):
    return [
        across_rows(face_blocks[1], 1),
        across_rows(face_blocks[0], -1),
        across_cols(face_blocks[3], 1),
        across_cols(face_blocks[2], -1),
        across_segment(face_blocks[5], 1),
        across_segment(face_blocks[4], -1),
    ]


def shards(
    node_latent,
    edge_latent,
    adjacency,
    neighbours,
    live,
    send_blocks,
    w_edge_in,
    w_edge_out,
    w_node_in,
    w_node_out,
    node_cotangent,
    edge_cotangent,
):
    latent = node_latent.shape[1]
    blocks, degree = neighbours.shape
    block_rows = adjacency.shape[-1]
    node_blocks = node_latent.reshape(blocks, block_rows, latent)
    choose = (send_blocks[0][:, None] == jnp.arange(blocks, dtype=jnp.int32)[None, :]).astype(
        jnp.bfloat16
    )
    outgoing = jnp.einsum(
        "jn,nbd->jbd", choose, node_blocks, preferred_element_type=jnp.float32
    ).astype(jnp.bfloat16)
    received = swap_faces(outgoing)
    adjacency_tiles = adjacency.reshape(blocks * degree, block_rows, block_rows)
    picker = (
        neighbours.reshape(-1)[:, None] == jnp.arange(blocks + 6, dtype=jnp.int32)[None, :]
    ).astype(jnp.bfloat16)
    live_weight = live.astype(jnp.float32)
    messages, edge_pull = jax.vjp(
        partial(edge_part, edge_rows=edge_latent, adjacency_tiles=adjacency_tiles, picker=picker),
        node_blocks,
        received,
        w_edge_in,
        w_edge_out,
    )
    outputs, node_pull = jax.vjp(
        partial(node_part, edge_rows=edge_latent, live_weight=live_weight),
        node_blocks,
        messages,
        w_node_in,
        w_node_out,
    )
    node_direct, message_ct, grad_ni, grad_no = node_pull((node_cotangent, edge_cotangent))
    node_terms = (grad_ni.astype(jnp.float32).reshape(-1), grad_no.astype(jnp.float32).reshape(-1))
    node_indirect, received_ct, grad_ei, grad_eo = edge_pull(message_ct)
    devices = 1 << len(INDEX_BITS)
    node_share = halving_scatter(
        jnp.concatenate([term.reshape(devices, -1) for term in node_terms], axis=1), NODE_ORDER
    )
    node_share, received_ct = lax.optimization_barrier((node_share, received_ct))
    returned = swap_faces(received_ct)
    node_grad = node_direct.astype(jnp.float32) + node_indirect.astype(jnp.float32)
    for face, block in enumerate(returned):
        node_grad = node_grad + choose[face].astype(jnp.float32)[:, None, None] * block.astype(
            jnp.float32
        )
    edge_terms = (grad_ei.astype(jnp.float32).reshape(-1), grad_eo.astype(jnp.float32).reshape(-1))
    devices = 1 << len(INDEX_BITS)
    edge_share = halving_scatter(
        jnp.concatenate([term.reshape(devices, -1) for term in edge_terms], axis=1), EDGE_ORDER
    )
    edge_cut = edge_terms[0].shape[0] // devices
    node_cut = node_terms[0].shape[0] // devices
    shares = (
        edge_share[:edge_cut],
        edge_share[edge_cut:],
        node_share[:node_cut],
        node_share[node_cut:],
    )
    return (
        outputs[0],
        outputs[1],
        node_grad.reshape(-1, latent),
        shares[0],
        shares[1],
        shares[2],
        shares[3],
    )


def solution(mesh):
    placed = (
        P(("segment", "gx", "gy"), None),
        P(("segment", "gx", "gy"), None),
        P(("segment", "gx", "gy"), None, None, None),
        P(("segment", "gx", "gy"), None),
        P(("segment", "gx", "gy"), None),
        P(("segment", "gx", "gy"), None),
        P(),
        P(),
        P(),
        P(),
        P(("segment", "gx", "gy"), None),
        P(("segment", "gx", "gy"), None),
    )
    return jax.shard_map(
        shards,
        mesh=mesh,
        in_specs=placed,
        out_specs=(
            P(("segment", "gx", "gy"), None),
            P(("segment", "gx", "gy"), None),
            P(("segment", "gx", "gy"), None),
            P(("segment", "gx", "gy")),
            P(("segment", "gx", "gy")),
            P(("segment", "gx", "gy")),
            P(("segment", "gx", "gy")),
        ),
        check_vma=False,
    )
```

```python
from functools import partial

import jax
import jax.numpy as jnp
from jax import lax
from jax.sharding import PartitionSpec as P


def passed_along(block, axis, distance):
    devices = range(lax.axis_size(axis))
    route = [(i - distance, i) for i in devices if i - distance in devices]
    return lax.ppermute(block, axis, route)


INDEX_BITS = (("segment", 0), ("gx", 2), ("gx", 1), ("gx", 0), ("gy", 3), ("gy", 2), ("gy", 1), ("gy", 0))
EDGE_ORDER = (7, 2, 0, 6, 1, 5, 3, 4)
NODE_ORDER = (7, 6, 2, 0, 3, 5, 4, 1)

def halving_scatter(rows, order):
    bits = len(INDEX_BITS)
    parts = rows.reshape((2,) * bits + rows.shape[1:]).transpose(tuple(order) + (bits,))
    for position in order:
        axis, bit = INDEX_BITS[position]
        side = (lax.axis_index(axis) >> bit) & 1
        route = [(j, j ^ (1 << bit)) for j in range(lax.axis_size(axis))]
        keep = lax.dynamic_index_in_dim(parts, side, 0, keepdims=False)
        send = lax.dynamic_index_in_dim(parts, 1 - side, 0, keepdims=False)
        arrived = lax.ppermute(send.astype(jnp.bfloat16), axis, route)
        parts = keep + arrived.astype(jnp.float32)
    return parts


def layer_norm(values):
    average = jnp.mean(values, axis=-1, keepdims=True)
    centred = values - average
    return centred * lax.rsqrt(jnp.mean(centred * centred, axis=-1, keepdims=True) + 1e-05)


def edge_part(node_blocks, received, w_edge_in, w_edge_out, edge_rows, adjacency_tiles, picker):
    latent = node_blocks.shape[-1]
    blocks = node_blocks.shape[0]
    block_rows = node_blocks.shape[1]
    degree = picker.shape[0] // blocks
    extended = jnp.concatenate([node_blocks] + [block[None] for block in received], axis=0)
    sources = jnp.einsum(
        "sn,nbd->sbd", picker, extended, preferred_element_type=jnp.float32
    ).astype(jnp.bfloat16)
    mixed_rows = jnp.einsum(
        "sij,sjd->sid", adjacency_tiles, sources, preferred_element_type=jnp.float32
    ).astype(jnp.bfloat16)
    self_term = jnp.dot(
        node_blocks.reshape(-1, latent),
        w_edge_in[latent : 2 * latent],
        preferred_element_type=jnp.float32,
    )
    pre_edge = jnp.dot(edge_rows, w_edge_in[:latent], preferred_element_type=jnp.float32) + jnp.dot(
        mixed_rows.reshape(-1, latent), w_edge_in[2 * latent :], preferred_element_type=jnp.float32
    )
    pre_edge = (
        pre_edge.reshape(blocks, degree, block_rows, latent)
        + self_term.reshape(blocks, 1, block_rows, latent)
    ).reshape(-1, latent)
    edge_hidden = jax.nn.silu(pre_edge).astype(jnp.bfloat16)
    return layer_norm(jnp.dot(edge_hidden, w_edge_out, preferred_element_type=jnp.float32))


def node_part(node_blocks, messages, w_node_in, w_node_out, edge_rows, live_weight):
    latent = node_blocks.shape[-1]
    blocks = node_blocks.shape[0]
    block_rows = node_blocks.shape[1]
    edges_out = (edge_rows.astype(jnp.float32) + messages).astype(jnp.bfloat16)
    gathered = jnp.sum(
        messages.reshape(blocks, -1, block_rows, latent) * live_weight[:, :, None, None], axis=1
    ).astype(jnp.bfloat16)
    flat_nodes = node_blocks.reshape(-1, latent)
    pre_node = jnp.dot(
        flat_nodes, w_node_in[:latent], preferred_element_type=jnp.float32
    ) + jnp.dot(
        gathered.reshape(-1, latent), w_node_in[latent:], preferred_element_type=jnp.float32
    )
    node_hidden = jax.nn.silu(pre_node).astype(jnp.bfloat16)
    nodes_out = (
        flat_nodes.astype(jnp.float32)
        + layer_norm(jnp.dot(node_hidden, w_node_out, preferred_element_type=jnp.float32))
    ).astype(jnp.bfloat16)
    return (nodes_out, edges_out)


def across_rows(face_rows, offset):
    return passed_along(face_rows, "gx", offset)


def across_cols(face_rows, offset):
    return passed_along(face_rows, "gy", offset)


def across_segment(face_rows, offset):
    return passed_along(face_rows, "segment", offset)


def swap_faces(face_blocks):
    return [
        across_rows(face_blocks[1], 1),
        across_rows(face_blocks[0], -1),
        across_cols(face_blocks[3], 1),
        across_cols(face_blocks[2], -1),
        across_segment(face_blocks[5], 1),
        across_segment(face_blocks[4], -1),
    ]


def shards(
    node_latent,
    edge_latent,
    adjacency,
    neighbours,
    live,
    send_blocks,
    w_edge_in,
    w_edge_out,
    w_node_in,
    w_node_out,
    node_cotangent,
    edge_cotangent,
):
    latent = node_latent.shape[1]
    blocks, degree = neighbours.shape
    block_rows = adjacency.shape[-1]
    node_blocks = node_latent.reshape(blocks, block_rows, latent)
    choose = (send_blocks[0][:, None] == jnp.arange(blocks, dtype=jnp.int32)[None, :]).astype(
        jnp.bfloat16
    )
    outgoing = jnp.einsum(
        "jn,nbd->jbd", choose, node_blocks, preferred_element_type=jnp.float32
    ).astype(jnp.bfloat16)
    received = swap_faces(outgoing)
    adjacency_tiles = adjacency.reshape(blocks * degree, block_rows, block_rows)
    picker = (
        neighbours.reshape(-1)[:, None] == jnp.arange(blocks + 6, dtype=jnp.int32)[None, :]
    ).astype(jnp.bfloat16)
    live_weight = live.astype(jnp.float32)
    messages, edge_pull = jax.vjp(
        partial(edge_part, edge_rows=edge_latent, adjacency_tiles=adjacency_tiles, picker=picker),
        node_blocks,
        received,
        w_edge_in,
        w_edge_out,
    )
    outputs, node_pull = jax.vjp(
        partial(node_part, edge_rows=edge_latent, live_weight=live_weight),
        node_blocks,
        messages,
        w_node_in,
        w_node_out,
    )
    node_direct, message_ct, grad_ni, grad_no = node_pull((node_cotangent, edge_cotangent))
    node_terms = (grad_ni.astype(jnp.float32).reshape(-1), grad_no.astype(jnp.float32).reshape(-1))
    node_indirect, received_ct, grad_ei, grad_eo = edge_pull(message_ct)
    returned = swap_faces(received_ct)
    node_grad = node_direct.astype(jnp.float32) + node_indirect.astype(jnp.float32)
    for face, block in enumerate(returned):
        node_grad = node_grad + choose[face].astype(jnp.float32)[:, None, None] * block.astype(
            jnp.float32
        )
    edge_terms = (grad_ei.astype(jnp.float32).reshape(-1), grad_eo.astype(jnp.float32).reshape(-1))
    devices = 1 << len(INDEX_BITS)
    edge_share = halving_scatter(
        jnp.concatenate([term.reshape(devices, -1) for term in edge_terms], axis=1), EDGE_ORDER
    )
    node_share = halving_scatter(
        jnp.concatenate([term.reshape(devices, -1) for term in node_terms], axis=1), NODE_ORDER
    )
    edge_cut = edge_terms[0].shape[0] // devices
    node_cut = node_terms[0].shape[0] // devices
    shares = (
        edge_share[:edge_cut],
        edge_share[edge_cut:],
        node_share[:node_cut],
        node_share[node_cut:],
    )
    return (
        outputs[0],
        outputs[1],
        node_grad.reshape(-1, latent),
        shares[0],
        shares[1],
        shares[2],
        shares[3],
    )


def solution(mesh):
    placed = (
        P(("segment", "gx", "gy"), None),
        P(("segment", "gx", "gy"), None),
        P(("segment", "gx", "gy"), None, None, None),
        P(("segment", "gx", "gy"), None),
        P(("segment", "gx", "gy"), None),
        P(("segment", "gx", "gy"), None),
        P(),
        P(),
        P(),
        P(),
        P(("segment", "gx", "gy"), None),
        P(("segment", "gx", "gy"), None),
    )
    return jax.shard_map(
        shards,
        mesh=mesh,
        in_specs=placed,
        out_specs=(
            P(("segment", "gx", "gy"), None),
            P(("segment", "gx", "gy"), None),
            P(("segment", "gx", "gy"), None),
            P(("segment", "gx", "gy")),
            P(("segment", "gx", "gy")),
            P(("segment", "gx", "gy")),
            P(("segment", "gx", "gy")),
        ),
        check_vma=False,
    )
```
